32 devices in a mesh: seq: 2 (over x), ctx: 8 (over z, y), wsh: 2 (over core).
Axes of the slice: x: 2, y: 2, z: 4, core: 2. Of those that a mesh axis runs over, the one named last changes fastest.
Arguments:
- layer_in: bfloat16 [2, 1024, 896], P('seq', 'ctx'), may hold values from -6 to 6
- grad_out: bfloat16 [2, 1024, 896], P('seq', 'ctx'), may hold values from -6 to 6
- positions: int32 [2, 1024], P('seq'), may hold values from 0 to 1023, as said below
- attn_gain: bfloat16 [896], P(('seq', 'ctx', 'wsh')), may hold values from 0.099609375 to 1.8984375
- w_query: bfloat16 [896, 896], P(('seq', 'ctx'), 'wsh'), may hold values from -0.1875 to 0.1875
- b_query: bfloat16 [896], P(('seq', 'ctx', 'wsh')), may hold values from -3 to 3
- w_keyvalue: bfloat16 [896, 256], P(('seq', 'ctx'), 'wsh'), may hold values from -0.1875 to 0.1875
- b_keyvalue: bfloat16 [256], P(('seq', 'ctx', 'wsh')), may hold values from -3 to 3
- w_output: bfloat16 [896, 896], P('wsh', ('seq', 'ctx')), may hold values from -3 to 3
- mlp_gain: bfloat16 [896], P(('seq', 'ctx', 'wsh')), may hold values from 0.099609375 to 1.8984375
- w_gate: bfloat16 [896, 4864], P(('seq', 'ctx'), 'wsh'), may hold values from -0.1875 to 0.1875
- w_up: bfloat16 [896, 4864], P(('seq', 'ctx'), 'wsh'), may hold values from -0.1875 to 0.1875
- w_down: bfloat16 [4864, 896], P('wsh', ('seq', 'ctx')), may hold values from -0.078125 to 0.078125
Outputs:
- layer_out: bfloat16 [2, 1024, 896], P('seq', 'ctx')
- grad_in: bfloat16 [2, 1024, 896], P('seq', 'ctx')
- grad_attn_gain: float32 [896], P(('seq', 'ctx', 'wsh'))
- grad_w_query: float32 [896, 896], P(('seq', 'ctx'), 'wsh')
- grad_b_query: float32 [896], P(('seq', 'ctx', 'wsh'))
- grad_w_keyvalue: float32 [896, 256], P(('seq', 'ctx'), 'wsh')
- grad_b_keyvalue: float32 [256], P(('seq', 'ctx', 'wsh'))
- grad_w_output: float32 [896, 896], P('wsh', ('seq', 'ctx'))
- grad_mlp_gain: float32 [896], P(('seq', 'ctx', 'wsh'))
- grad_w_gate: float32 [896, 4864], P(('seq', 'ctx'), 'wsh')
- grad_w_up: float32 [896, 4864], P(('seq', 'ctx'), 'wsh')
- grad_w_down: float32 [4864, 896], P('wsh', ('seq', 'ctx'))
The draws below stay inside these ranges and needn't reach their ends.
Inputs may be any that keep to these rules, and one draw needn't show every extreme that they name: Each row (one sequence) holds every position 0 to 1023 once; the 128 rows of one index of ctx are two blocks of 64 consecutive positions, block p then block 15 - p, with the pair p of each index drawn per sequence.
All inputs are finite; a program needn't handle non-finite values.
Results may differ from the reference program's by a relative error of at most 0.018.
Values may be sent and summed in bfloat16 or wider, within the bound.
No kernel may reach another device: no remote copies, remote signals or barrier semaphores. Data moves between devices by JAX's collectives and lax.ppermute only.
A program may use at most 192 MiB of HBM per device.

```python
import math
import jax
import jax.numpy as jnp
from jax import lax

D = 896
HQ = 14
KVH = 2
HD = 64
FF = 4864
BLK = 64
SEQS = 2
SEQLEN = 1024


def seq_order(seq_key):
    pair_count = SEQLEN // (2 * BLK)
    pair_order = jax.random.permutation(seq_key, pair_count).astype(jnp.int32)
    offsets = jnp.arange(BLK, dtype=jnp.int32)
    first_rows = pair_order[:, None] * BLK + offsets[None, :]
    second_rows = (2 * pair_count - 1 - pair_order)[:, None] * BLK + offsets[None, :]
    return jnp.concatenate([first_rows, second_rows], axis=1).reshape(SEQLEN).astype(jnp.int32)


def draw_positions(key, part):
    return jax.vmap(seq_order)(jax.random.split(key, SEQS))


def spiked(result, rng, source, target, shards_of, factor):
    def block_of(axis_at):
        return (jnp.arange(result.shape[axis_at]) // (result.shape[axis_at] // shards_of)).reshape((-1,) + (1,) * (result.ndim - 1 - axis_at))

    one_side = jax.random.permutation(rng, shards_of)[block_of(target)]
    other_side = (block_of(target) + shards_of // 2) % shards_of
    return jnp.where((block_of(source) == one_side) | (block_of(source) == other_side), factor * result, result)


def level_of(rng, dims, cuts, smallest, top_value):
    level, own = 1.0, jax.random.fold_in(rng, 6)
    for position, parts in cuts:
        draws = jnp.exp(jax.random.uniform(jax.random.fold_in(own, position), (parts,), jnp.float32, smallest / len(cuts), top_value / len(cuts)))
        level = level * jnp.repeat(draws, dims[position] // parts).reshape([-1 if axis == position else 1 for axis in range(len(dims))])
    return level


def bell_draw(rng, shape, width, most, pieces=(), kind=jnp.bfloat16):
    result = jax.random.normal(rng, shape, jnp.float32) * width
    if len(pieces) > 0:
        result = level_of(rng, shape, pieces, -0.22, 0.18) * result
    return jnp.clip(result, min=-most, max=most).astype(kind)


def heavy_noise(key, shape, width, most, shards, heavy, kind=jnp.bfloat16):
    values = width * jax.random.normal(key, shape, jnp.float32)
    if shards:
        values = values * level_of(key, shape, shards, -0.22, 0.18)
    return jnp.clip(spiked(values, jax.random.fold_in(key, 3), *heavy), -most, most).astype(kind)


def setup_inputs(seed: int = 0) -> dict:
    streams_of = jax.random.split(jax.random.key(seed), 14)
    return {
        "layer_in": bell_draw(streams_of[0], (SEQS, SEQLEN, D), 1.0, 6.0, ((0, 2), (1, 8))),
        "grad_out": heavy_noise(streams_of[1], (SEQS, SEQLEN, D), 1.0, 6.0, ((0, 2), (1, 8)), (1, 2, 8, 2.0)),
        "positions": draw_positions(jax.random.fold_in(streams_of[13], 71), 0),
        "attn_gain": jnp.clip(1.0 + 0.18 * jax.random.normal(streams_of[3], (D,), jnp.float32), 0.099609375, 1.8984375).astype(jnp.bfloat16),
        "w_query": bell_draw(streams_of[4], (D, HQ * HD), D ** -0.5, 0.1875, ((0, 16), (1, 2))),
        "b_query": bell_draw(streams_of[5], (HQ * HD,), 0.5, 3.0, ((0, 32),)),
        "w_keyvalue": bell_draw(streams_of[6], (D, 2 * KVH * HD), D ** -0.5, 0.1875, ((0, 16), (1, 2))),
        "b_keyvalue": bell_draw(streams_of[7], (2 * KVH * HD,), 0.5, 3.0, ((0, 32),)),
        "w_output": bell_draw(streams_of[8], (HQ * HD, D), 4 ** -0.5, 3.0, ((0, 2), (1, 16))),
        "mlp_gain": jnp.clip(1.0 + 0.18 * jax.random.normal(streams_of[9], (D,), jnp.float32), 0.099609375, 1.8984375).astype(jnp.bfloat16),
        "w_gate": bell_draw(streams_of[10], (D, FF), D ** -0.5, 0.1875, ((0, 16), (1, 2))),
        "w_up": bell_draw(streams_of[11], (D, FF), D ** -0.5, 0.1875, ((0, 16), (1, 2))),
        "w_down": bell_draw(streams_of[12], (FF, D), FF ** -0.5, 0.078125, ((0, 2), (1, 16))),
    }


@jax.custom_vjp
def low(v):
    return lax.optimization_barrier(v.astype(jnp.bfloat16)).astype(jnp.float32)

@jax.custom_vjp
def low_back(v):
    return v

def low_keep(v):
    return (low(v), None)

def low_pass(kept, grad):
    return (grad,)

def back_keep(v):
    return (v, None)

def back_low(kept, grad):
    return (low(grad),)
low.defvjp(low_keep, low_pass)
low_back.defvjp(back_keep, back_low)
highest = lax.Precision.HIGHEST
epsilon = 1e-06
theta_log = math.log(1000000.0)

def matmul_hi(left_mat, right_mat):
    return jnp.dot(left_mat, right_mat, precision=highest)

def rms_scale(values):
    return lax.rsqrt(lax.optimization_barrier(jnp.mean(values * values, axis=-1, keepdims=True)) + epsilon)

def rope_tables(positions, half_dim):
    inv_freq = jnp.exp(-jnp.arange(half_dim, dtype=jnp.float32) * (theta_log / half_dim))
    turned = positions.astype(jnp.float32)[:, None] * inv_freq[None, :]
    return (jnp.cos(turned)[:, None, :], jnp.sin(turned)[:, None, :])

def rotate(values, cos_tab, sin_tab):
    half_dim = values.shape[-1] // 2
    first_half = values[..., :half_dim]
    second_half = values[..., half_dim:]
    return jnp.concatenate([first_half * cos_tab - second_half * sin_tab, second_half * cos_tab + first_half * sin_tab], axis=-1)

def forward_layer(x_seq, attn_gain, w_query, b_query, w_keyvalue, b_keyvalue, w_output, mlp_gain, w_gate, w_up, w_down, positions):
    seq_len = x_seq.shape[0]
    group_size = HQ // KVH
    score_scale = 1.0 / math.sqrt(HD)
    normed_one = low(x_seq * rms_scale(x_seq) * attn_gain)
    query_pre = low_back(matmul_hi(normed_one, w_query) + b_query)
    kv_pre = (matmul_hi(normed_one, w_keyvalue) + b_keyvalue).reshape(seq_len, KVH, 2, HD)
    key_pre = low_back(kv_pre[:, :, 0, :])
    value_low = low(low_back(kv_pre[:, :, 1, :]))
    cos_tab, sin_tab = rope_tables(positions, HD // 2)
    query_low = low(rotate(query_pre.reshape(seq_len, HQ, HD), cos_tab, sin_tab))
    key_low = low(rotate(key_pre, cos_tab, sin_tab))
    q_rows = math.gcd(seq_len, 512)

    def attend(q_pair):
        query_blk, pos_blk = q_pair
        query_grp = query_blk.reshape(q_rows, KVH, group_size, HD)
        scores = jnp.einsum('qgrd,kgd->grqk', query_grp, key_low, precision=highest) * score_scale
        scores = low_back(scores)
        allowed = positions[None, :] <= pos_blk[:, None]
        scores = jnp.where(allowed[None, None], scores, -1e+30)
        prob_low = low(jax.nn.softmax(scores, axis=-1))
        mixed = jnp.einsum('grqk,kgd->qgrd', prob_low, value_low, precision=highest)
        return mixed.reshape(q_rows, HQ * HD)
    attended = lax.map(jax.checkpoint(attend), (query_low.reshape(seq_len // q_rows, q_rows, HQ, HD), positions.reshape(seq_len // q_rows, q_rows)))
    attended = low(low_back(attended.reshape(seq_len, HQ * HD)))
    branch = low_back(matmul_hi(attended, w_output))
    hidden = x_seq + branch
    normed_two = low(hidden * rms_scale(hidden) * mlp_gain)
    gate_pre = low_back(matmul_hi(normed_two, w_gate))
    up_proj = low_back(matmul_hi(normed_two, w_up))
    act_low = low(jax.nn.silu(gate_pre) * up_proj)
    return hidden + matmul_hi(act_low, w_down)

def reference(layer_in, grad_out, positions, attn_gain, w_query, b_query, w_keyvalue, b_keyvalue, w_output, mlp_gain, w_gate, w_up, w_down):
    weights_f = [tensor.astype(jnp.float32) for tensor in (attn_gain, w_query, b_query, w_keyvalue, b_keyvalue, w_output, mlp_gain, w_gate, w_up, w_down)]
    summed = [jnp.zeros_like(tensor) for tensor in weights_f]
    outputs = []
    in_grads = []
    for seq_index in range(layer_in.shape[0]):
        seq_pos = positions[seq_index]

        def layer_fn(x_seq, g_one, w_q, b_q, w_kv, b_kv, w_o, g_two, w_g, w_u, w_d):
            return forward_layer(x_seq, g_one, w_q, b_q, w_kv, b_kv, w_o, g_two, w_g, w_u, w_d, seq_pos)
        out_seq, pull_back = jax.vjp(layer_fn, layer_in[seq_index].astype(jnp.float32), weights_f[0], weights_f[1], weights_f[2], weights_f[3], weights_f[4], weights_f[5], weights_f[6], weights_f[7], weights_f[8], weights_f[9])
        grad_list = pull_back(grad_out[seq_index].astype(jnp.float32))
        outputs.append(out_seq.astype(jnp.bfloat16))
        in_grads.append(grad_list[0].astype(jnp.bfloat16))
        summed = [acc_sum + g_part for acc_sum, g_part in zip(summed, grad_list[1:])]
    return (jnp.stack(outputs), jnp.stack(in_grads), summed[0], summed[1], summed[2], summed[3], summed[4], summed[5], summed[6], summed[7], summed[8], summed[9])
```

```python
import math

import jax
import jax.numpy as jnp
from jax import lax
from jax.sharding import PartitionSpec as P

HD = 64


epsilon = 1e-06
theta_log = math.log(1000000.0)


def partner(block, axis, stride):
    count = lax.axis_size(axis)
    route = []
    for low in range(count):
        high = low | 1 << stride
        if high != low and high < count:
            route += [(low, high), (high, low)]
    return lax.ppermute(block, axis, route)


def rope_tables(positions, half_dim):
    inv_freq = jnp.exp(-jnp.arange(half_dim, dtype=jnp.float32) * (theta_log / half_dim))
    turned = positions.astype(jnp.float32)[:, None] * inv_freq[None, :]
    return (jnp.cos(turned)[:, None, :], jnp.sin(turned)[:, None, :])


def rotate(values, cos_tab, sin_tab):
    half_dim = values.shape[-1] // 2
    first_half = values[..., :half_dim]
    second_half = values[..., half_dim:]
    return jnp.concatenate(
        [
            first_half * cos_tab - second_half * sin_tab,
            second_half * cos_tab + first_half * sin_tab,
        ],
        axis=-1,
    )


def left_inner(left_mat, right_mat):
    return lax.dot_general(
        left_mat, right_mat, (((0,), (0,)), ((), ())), preferred_element_type=jnp.float32
    )


def right_inner(left_mat, right_mat):
    return lax.dot_general(
        left_mat, right_mat, (((1,), (1,)), ((), ())), preferred_element_type=jnp.float32
    )


def norm_back(grad_normed, normed_hat, scale_inv, gain_vec):
    weighted = grad_normed * gain_vec
    return scale_inv * (
        weighted - normed_hat * jnp.mean(weighted * normed_hat, axis=-1, keepdims=True)
    )


def halve_sum(buffer, sender, group_count, group_index):
    for bit_pos in reversed(range(group_count.bit_length() - 1)):
        half_rows = buffer.shape[0] // 2
        my_bit = group_index >> bit_pos & 1
        kept_rows = lax.dynamic_slice_in_dim(buffer, my_bit * half_rows, half_rows, 0)
        outgoing = lax.dynamic_slice_in_dim(buffer, (1 - my_bit) * half_rows, half_rows, 0)
        buffer = kept_rows + sender(outgoing, bit_pos)
    return buffer


def per_device(
    layer_in,
    grad_out,
    positions,
    attn_gain,
    w_query,
    b_query,
    w_keyvalue,
    b_keyvalue,
    w_output,
    mlp_gain,
    w_gate,
    w_up,
    w_down,
):
    wq_full, wkv_full, wo_full, wg_full, wu_full, wd_full = (
        lax.all_gather(w_query, ("seq", "ctx"), axis=0, tiled=True),
        lax.all_gather(w_keyvalue, ("seq", "ctx"), axis=0, tiled=True),
        lax.all_gather(w_output, ("seq", "ctx"), axis=1, tiled=True),
        lax.all_gather(w_gate, ("seq", "ctx"), axis=0, tiled=True),
        lax.all_gather(w_up, ("seq", "ctx"), axis=0, tiled=True),
        lax.all_gather(w_down, ("seq", "ctx"), axis=1, tiled=True),
    )
    g_one, bias_q, bias_kv, g_two = (
        lax.all_gather(attn_gain, ("seq", "ctx", "wsh"), axis=0, tiled=True),
        lax.all_gather(b_query, ("seq", "ctx", "wsh"), axis=0, tiled=True),
        lax.all_gather(b_keyvalue, ("seq", "ctx", "wsh"), axis=0, tiled=True),
        lax.all_gather(mlp_gain, ("seq", "ctx", "wsh"), axis=0, tiled=True),
    )
    shard_id = lax.axis_index("wsh")
    group_count = lax.axis_size(("seq", "ctx"))
    group_index = lax.axis_index(("seq", "ctx"))
    q_cols = wq_full.shape[1]
    kv_cols = wkv_full.shape[1]
    ff_cols = wg_full.shape[1]
    bias_q = lax.dynamic_slice_in_dim(bias_q, shard_id * q_cols, q_cols).astype(jnp.float32)
    bias_kv = lax.dynamic_slice_in_dim(bias_kv, shard_id * kv_cols, kv_cols).astype(jnp.float32)
    g_one = g_one.astype(jnp.float32)
    g_two = g_two.astype(jnp.float32)
    row_count = layer_in.shape[1]
    head_count = q_cols // HD
    seq_len = positions.shape[1]
    score_scale = 1.0 / math.sqrt(HD)
    pos_all = positions[0]
    pos_mine = lax.dynamic_slice_in_dim(pos_all, lax.axis_index("ctx") * row_count, row_count)
    x_full = layer_in[0].astype(jnp.float32)
    scale_one = lax.rsqrt(jnp.mean(x_full * x_full, axis=-1, keepdims=True) + epsilon)
    hat_one = x_full * scale_one
    normed_one = (hat_one * g_one).astype(jnp.bfloat16)
    query_pre = jnp.dot(normed_one, wq_full, preferred_element_type=jnp.float32) + bias_q
    kv_pre = jnp.dot(normed_one, wkv_full, preferred_element_type=jnp.float32) + bias_kv
    cos_tab, sin_tab = rope_tables(pos_mine, HD // 2)
    query_low = rotate(query_pre.reshape(row_count, head_count, HD), cos_tab, sin_tab).astype(
        jnp.bfloat16
    )
    key_low = rotate(kv_pre[:, None, :HD], cos_tab, sin_tab)[:, 0, :].astype(jnp.bfloat16)
    value_low = kv_pre[:, HD:].astype(jnp.bfloat16)
    kv_all = lax.all_gather(
        jnp.concatenate([key_low, value_low], axis=1), "ctx", axis=0, tiled=True
    )
    k_rows = math.gcd(seq_len, 512)
    blocks_n = seq_len // k_rows
    kv_blocks = kv_all.reshape(blocks_n, k_rows, 2 * HD)
    pos_blocks = pos_all.reshape(blocks_n, k_rows)

    def block_scores(kv_block, pos_block):
        scores = (
            jnp.einsum(
                "qhd,kd->hqk", query_low, kv_block[:, :HD], preferred_element_type=jnp.float32
            )
            * score_scale
        )
        allowed = pos_block[None, :] <= pos_mine[:, None]
        return jnp.where(allowed[None], scores, -1e30)

    def stats_step(run_state, kv_pair):
        run_max, run_sum = run_state
        scores = block_scores(kv_pair[0], kv_pair[1])
        new_max = jnp.maximum(run_max, jnp.max(scores, axis=-1))
        run_sum = run_sum * jnp.exp(run_max - new_max) + jnp.sum(
            jnp.exp(scores - new_max[..., None]), axis=-1
        )
        return ((new_max, run_sum), None)

    init_max = jnp.full((head_count, row_count), -1e30, jnp.float32)
    init_sum = jnp.zeros((head_count, row_count), jnp.float32)
    (run_max, run_sum), unused = lax.scan(stats_step, (init_max, init_sum), (kv_blocks, pos_blocks))
    log_sum = run_max + jnp.log(run_sum)

    def out_step(run_state, kv_pair):
        sum_low, sum_full = run_state
        scores = block_scores(kv_pair[0], kv_pair[1])
        prob_full = jnp.exp(scores - log_sum[..., None])
        prob_low = prob_full.astype(jnp.bfloat16)
        value_blk = kv_pair[0][:, HD:]
        sum_low = sum_low + jnp.einsum(
            "hqk,kd->hqd", prob_low, value_blk, preferred_element_type=jnp.float32
        )
        sum_full = sum_full + jnp.einsum(
            "hqk,kd->hqd",
            prob_full,
            value_blk.astype(jnp.float32),
            preferred_element_type=jnp.float32,
        )
        return ((sum_low, sum_full), None)

    zero_heads = jnp.zeros((head_count, row_count, HD), jnp.float32)
    (attended, attended_exact), unused = lax.scan(
        out_step, (zero_heads, zero_heads), (kv_blocks, pos_blocks)
    )
    attended_low = (
        jnp.transpose(attended, (1, 0, 2)).reshape(row_count, head_count * HD).astype(jnp.bfloat16)
    )
    branch = lax.psum(jnp.dot(attended_low, wo_full, preferred_element_type=jnp.float32), "wsh")
    hidden = x_full + branch
    scale_two = lax.rsqrt(jnp.mean(hidden * hidden, axis=-1, keepdims=True) + epsilon)
    hat_two = hidden * scale_two
    normed_two = (hat_two * g_two).astype(jnp.bfloat16)
    gate_pre = jnp.dot(normed_two, wg_full, preferred_element_type=jnp.float32)
    up_proj = jnp.dot(normed_two, wu_full, preferred_element_type=jnp.float32)
    act_low = (jax.nn.silu(gate_pre) * up_proj).astype(jnp.bfloat16)
    mlp_out = lax.psum(
        jnp.dot(act_low, wd_full, preferred_element_type=jnp.float32).astype(jnp.bfloat16), "wsh"
    ).astype(jnp.float32)
    layer_out = (hidden + mlp_out).astype(jnp.bfloat16)
    wq_full, wkv_full, wo_full, wg_full, wu_full, wd_full = (
        lax.all_gather(w_query, ("seq", "ctx"), axis=0, tiled=True),
        lax.all_gather(w_keyvalue, ("seq", "ctx"), axis=0, tiled=True),
        lax.all_gather(w_output, ("seq", "ctx"), axis=1, tiled=True),
        lax.all_gather(w_gate, ("seq", "ctx"), axis=0, tiled=True),
        lax.all_gather(w_up, ("seq", "ctx"), axis=0, tiled=True),
        lax.all_gather(w_down, ("seq", "ctx"), axis=1, tiled=True),
    )
    grad_low = grad_out[0]
    grad_full = grad_low.astype(jnp.float32)
    grad_act = right_inner(grad_low, wd_full)
    gw_down_t = left_inner(grad_low, act_low)
    sigmoid_g = jax.nn.sigmoid(gate_pre)
    grad_up = (grad_act * (gate_pre * sigmoid_g)).astype(jnp.bfloat16)
    grad_gate = (grad_act * up_proj * sigmoid_g * (1.0 + gate_pre * (1.0 - sigmoid_g))).astype(
        jnp.bfloat16
    )
    gw_gate = left_inner(normed_two, grad_gate)
    gw_up = left_inner(normed_two, grad_up)
    part_two = right_inner(grad_gate, wg_full) + right_inner(grad_up, wu_full)
    gg_two = jnp.sum(part_two * hat_two, axis=0)
    grad_normed_two = lax.psum(part_two.astype(jnp.bfloat16), "wsh").astype(jnp.float32)
    grad_hidden = grad_full + norm_back(grad_normed_two, hat_two, scale_two, g_two)
    hidden_low = grad_hidden.astype(jnp.bfloat16)
    gw_out_t = left_inner(hidden_low, attended_low)
    grad_att = (
        right_inner(hidden_low, wo_full).reshape(row_count, head_count, HD).astype(jnp.bfloat16)
    )
    row_delta = jnp.sum(
        jnp.transpose(grad_att.astype(jnp.float32), (1, 0, 2)) * attended_exact, axis=-1
    )

    def back_step(grad_q, kv_pair):
        kv_block, pos_block = kv_pair
        scores = block_scores(kv_block, pos_block)
        prob_full = jnp.exp(scores - log_sum[..., None])
        prob_low = prob_full.astype(jnp.bfloat16)
        grad_prob = jnp.einsum(
            "qhd,kd->hqk", grad_att, kv_block[:, HD:], preferred_element_type=jnp.float32
        )
        grad_score = (prob_full * (grad_prob - row_delta[..., None])).astype(jnp.bfloat16)
        grad_q = grad_q + jnp.einsum(
            "hqk,kd->qhd", grad_score, kv_block[:, :HD], preferred_element_type=jnp.float32
        )
        grad_key = jnp.einsum(
            "hqk,qhd->kd", grad_score, query_low, preferred_element_type=jnp.float32
        )
        grad_value = jnp.einsum(
            "hqk,qhd->kd", prob_low, grad_att, preferred_element_type=jnp.float32
        )
        return (grad_q, jnp.concatenate([grad_key * score_scale, grad_value], axis=1))

    grad_q, kv_terms = lax.scan(
        back_step, jnp.zeros((row_count, head_count, HD), jnp.float32), (kv_blocks, pos_blocks)
    )
    grad_q = grad_q * score_scale
    grad_kv = lax.psum_scatter(
        kv_terms.reshape(seq_len, 2 * HD).astype(jnp.bfloat16),
        "ctx",
        scatter_dimension=0,
        tiled=True,
    ).astype(jnp.float32)
    grad_qpre = (
        rotate(grad_q, cos_tab, -sin_tab).reshape(row_count, head_count * HD).astype(jnp.bfloat16)
    )
    grad_kpre = rotate(grad_kv[:, None, :HD], cos_tab, -sin_tab)[:, 0, :]
    grad_kvpre = jnp.concatenate([grad_kpre, grad_kv[:, HD:]], axis=1).astype(jnp.bfloat16)
    gw_query = left_inner(normed_one, grad_qpre)
    gw_kv = left_inner(normed_one, grad_kvpre)
    wsh_count = lax.axis_size("wsh")
    gb_q_full = lax.dynamic_update_slice_in_dim(
        jnp.zeros((q_cols * wsh_count,), jnp.float32),
        jnp.sum(grad_qpre.astype(jnp.float32), axis=0),
        shard_id * q_cols,
        0,
    )
    gb_kv_full = lax.dynamic_update_slice_in_dim(
        jnp.zeros((kv_cols * wsh_count,), jnp.float32),
        jnp.sum(grad_kvpre.astype(jnp.float32), axis=0),
        shard_id * kv_cols,
        0,
    )
    part_one = right_inner(grad_qpre, wq_full) + right_inner(grad_kvpre, wkv_full)
    gg_one = jnp.sum(part_one * hat_one, axis=0)
    grad_normed_one = lax.psum(part_one.astype(jnp.bfloat16), "wsh").astype(jnp.float32)
    grad_input = (grad_hidden + norm_back(grad_normed_one, hat_one, scale_one, g_one)).astype(
        jnp.bfloat16
    )
    out_g_one, out_b_q, out_b_kv, out_g_two = (
        lax.psum_scatter(gg_one, ("seq", "ctx", "wsh"), scatter_dimension=0, tiled=True),
        lax.psum_scatter(gb_q_full, ("seq", "ctx", "wsh"), scatter_dimension=0, tiled=True),
        lax.psum_scatter(gb_kv_full, ("seq", "ctx", "wsh"), scatter_dimension=0, tiled=True),
        lax.psum_scatter(gg_two, ("seq", "ctx", "wsh"), scatter_dimension=0, tiled=True),
    )
    all_owned = lax.psum_scatter(
        jnp.concatenate(
            [gw_query, gw_kv, gw_out_t, gw_gate, gw_up, gw_down_t], axis=1
        ).astype(jnp.bfloat16),
        ("seq", "ctx"),
        scatter_dimension=0,
        tiled=True,
    ).astype(jnp.float32)
    proj_owned = all_owned[:, : 2 * q_cols + kv_cols]
    mlp_owned = all_owned[:, 2 * q_cols + kv_cols :]
    out_wq = proj_owned[:, :q_cols]
    out_wkv = proj_owned[:, q_cols : q_cols + kv_cols]
    out_wo = jnp.transpose(proj_owned[:, q_cols + kv_cols :])
    out_wg = mlp_owned[:, :ff_cols]
    out_wu = mlp_owned[:, ff_cols : 2 * ff_cols]
    out_wd = jnp.transpose(mlp_owned[:, 2 * ff_cols :])
    return (
        layer_out[None],
        grad_input[None],
        out_g_one,
        out_wq,
        out_b_q,
        out_wkv,
        out_b_kv,
        out_wo,
        out_g_two,
        out_wg,
        out_wu,
        out_wd,
    )


def solution(mesh):
    return jax.shard_map(
        per_device,
        mesh=mesh,
        in_specs=(
            P("seq", "ctx", None),
            P("seq", "ctx", None),
            P("seq", None),
            P(("seq", "ctx", "wsh")),
            P(("seq", "ctx"), "wsh"),
            P(("seq", "ctx", "wsh")),
            P(("seq", "ctx"), "wsh"),
            P(("seq", "ctx", "wsh")),
            P("wsh", ("seq", "ctx")),
            P(("seq", "ctx", "wsh")),
            P(("seq", "ctx"), "wsh"),
            P(("seq", "ctx"), "wsh"),
            P("wsh", ("seq", "ctx")),
        ),
        out_specs=(
            P("seq", "ctx", None),
            P("seq", "ctx", None),
            P(("seq", "ctx", "wsh")),
            P(("seq", "ctx"), "wsh"),
            P(("seq", "ctx", "wsh")),
            P(("seq", "ctx"), "wsh"),
            P(("seq", "ctx", "wsh")),
            P("wsh", ("seq", "ctx")),
            P(("seq", "ctx", "wsh")),
            P(("seq", "ctx"), "wsh"),
            P(("seq", "ctx"), "wsh"),
            P("wsh", ("seq", "ctx")),
        ),
        check_vma=False,
    )
```

```python
import math

import jax
import jax.numpy as jnp
from jax import lax
from jax.sharding import PartitionSpec as P

HD = 64


epsilon = 1e-06
theta_log = math.log(1000000.0)


def partner(block, axis, stride):
    count = lax.axis_size(axis)
    route = []
    for low in range(count):
        high = low | 1 << stride
        if high != low and high < count:
            route += [(low, high), (high, low)]
    return lax.ppermute(block, axis, route)


def rope_tables(positions, half_dim):
    inv_freq = jnp.exp(-jnp.arange(half_dim, dtype=jnp.float32) * (theta_log / half_dim))
    turned = positions.astype(jnp.float32)[:, None] * inv_freq[None, :]
    return (jnp.cos(turned)[:, None, :], jnp.sin(turned)[:, None, :])


def rotate(values, cos_tab, sin_tab):
    half_dim = values.shape[-1] // 2
    first_half = values[..., :half_dim]
    second_half = values[..., half_dim:]
    return jnp.concatenate(
        [
            first_half * cos_tab - second_half * sin_tab,
            second_half * cos_tab + first_half * sin_tab,
        ],
        axis=-1,
    )


def left_inner(left_mat, right_mat):
    return lax.dot_general(
        left_mat, right_mat, (((0,), (0,)), ((), ())), preferred_element_type=jnp.float32
    )


def right_inner(left_mat, right_mat):
    return lax.dot_general(
        left_mat, right_mat, (((1,), (1,)), ((), ())), preferred_element_type=jnp.float32
    )


def norm_back(grad_normed, normed_hat, scale_inv, gain_vec):
    weighted = grad_normed * gain_vec
    return scale_inv * (
        weighted - normed_hat * jnp.mean(weighted * normed_hat, axis=-1, keepdims=True)
    )


def halve_sum(buffer, sender, group_count, group_index):
    for bit_pos in reversed(range(group_count.bit_length() - 1)):
        half_rows = buffer.shape[0] // 2
        my_bit = group_index >> bit_pos & 1
        kept_rows = lax.dynamic_slice_in_dim(buffer, my_bit * half_rows, half_rows, 0)
        outgoing = lax.dynamic_slice_in_dim(buffer, (1 - my_bit) * half_rows, half_rows, 0)
        buffer = kept_rows + sender(outgoing, bit_pos)
    return buffer


def per_device(
    layer_in,
    grad_out,
    positions,
    attn_gain,
    w_query,
    b_query,
    w_keyvalue,
    b_keyvalue,
    w_output,
    mlp_gain,
    w_gate,
    w_up,
    w_down,
):
    wq_full, wkv_full, wo_full, wg_full, wu_full, wd_full = (
        lax.all_gather(w_query, ("seq", "ctx"), axis=0, tiled=True),
        lax.all_gather(w_keyvalue, ("seq", "ctx"), axis=0, tiled=True),
        lax.all_gather(w_output, ("seq", "ctx"), axis=1, tiled=True),
        lax.all_gather(w_gate, ("seq", "ctx"), axis=0, tiled=True),
        lax.all_gather(w_up, ("seq", "ctx"), axis=0, tiled=True),
        lax.all_gather(w_down, ("seq", "ctx"), axis=1, tiled=True),
    )
    g_one, bias_q, bias_kv, g_two = (
        lax.all_gather(attn_gain, ("seq", "ctx", "wsh"), axis=0, tiled=True),
        lax.all_gather(b_query, ("seq", "ctx", "wsh"), axis=0, tiled=True),
        lax.all_gather(b_keyvalue, ("seq", "ctx", "wsh"), axis=0, tiled=True),
        lax.all_gather(mlp_gain, ("seq", "ctx", "wsh"), axis=0, tiled=True),
    )
    shard_id = lax.axis_index("wsh")
    group_count = lax.axis_size(("seq", "ctx"))
    group_index = lax.axis_index(("seq", "ctx"))
    q_cols = wq_full.shape[1]
    kv_cols = wkv_full.shape[1]
    ff_cols = wg_full.shape[1]
    bias_q = lax.dynamic_slice_in_dim(bias_q, shard_id * q_cols, q_cols).astype(jnp.float32)
    bias_kv = lax.dynamic_slice_in_dim(bias_kv, shard_id * kv_cols, kv_cols).astype(jnp.float32)
    g_one = g_one.astype(jnp.float32)
    g_two = g_two.astype(jnp.float32)
    row_count = layer_in.shape[1]
    head_count = q_cols // HD
    seq_len = positions.shape[1]
    score_scale = 1.0 / math.sqrt(HD)
    pos_all = positions[0]
    pos_mine = lax.dynamic_slice_in_dim(pos_all, lax.axis_index("ctx") * row_count, row_count)
    x_full = layer_in[0].astype(jnp.float32)
    scale_one = lax.rsqrt(jnp.mean(x_full * x_full, axis=-1, keepdims=True) + epsilon)
    hat_one = x_full * scale_one
    normed_one = (hat_one * g_one).astype(jnp.bfloat16)
    query_pre = jnp.dot(normed_one, wq_full, preferred_element_type=jnp.float32) + bias_q
    kv_pre = jnp.dot(normed_one, wkv_full, preferred_element_type=jnp.float32) + bias_kv
    cos_tab, sin_tab = rope_tables(pos_mine, HD // 2)
    query_low = rotate(query_pre.reshape(row_count, head_count, HD), cos_tab, sin_tab).astype(
        jnp.bfloat16
    )
    key_low = rotate(kv_pre[:, None, :HD], cos_tab, sin_tab)[:, 0, :].astype(jnp.bfloat16)
    value_low = kv_pre[:, HD:].astype(jnp.bfloat16)
    kv_all = lax.all_gather(
        jnp.concatenate([key_low, value_low], axis=1), "ctx", axis=0, tiled=True
    )
    k_rows = math.gcd(seq_len, 512)
    blocks_n = seq_len // k_rows
    kv_blocks = kv_all.reshape(blocks_n, k_rows, 2 * HD)
    pos_blocks = pos_all.reshape(blocks_n, k_rows)

    def block_scores(kv_block, pos_block):
        scores = (
            jnp.einsum(
                "qhd,kd->hqk", query_low, kv_block[:, :HD], preferred_element_type=jnp.float32
            )
            * score_scale
        )
        allowed = pos_block[None, :] <= pos_mine[:, None]
        return jnp.where(allowed[None], scores, -1e30)

    def stats_step(run_state, kv_pair):
        run_max, run_sum = run_state
        scores = block_scores(kv_pair[0], kv_pair[1])
        new_max = jnp.maximum(run_max, jnp.max(scores, axis=-1))
        run_sum = run_sum * jnp.exp(run_max - new_max) + jnp.sum(
            jnp.exp(scores - new_max[..., None]), axis=-1
        )
        return ((new_max, run_sum), None)

    init_max = jnp.full((head_count, row_count), -1e30, jnp.float32)
    init_sum = jnp.zeros((head_count, row_count), jnp.float32)
    (run_max, run_sum), unused = lax.scan(
        stats_step, (init_max, init_sum), (kv_blocks, pos_blocks), unroll=True
    )
    log_sum = run_max + jnp.log(run_sum)

    def out_step(run_state, kv_pair):
        sum_low, sum_full = run_state
        scores = block_scores(kv_pair[0], kv_pair[1])
        prob_full = jnp.exp(scores - log_sum[..., None])
        prob_low = prob_full.astype(jnp.bfloat16)
        value_blk = kv_pair[0][:, HD:]
        sum_low = sum_low + jnp.einsum(
            "hqk,kd->hqd", prob_low, value_blk, preferred_element_type=jnp.float32
        )
        sum_full = sum_full + jnp.einsum(
            "hqk,kd->hqd",
            prob_full,
            value_blk.astype(jnp.float32),
            preferred_element_type=jnp.float32,
        )
        return ((sum_low, sum_full), None)

    zero_heads = jnp.zeros((head_count, row_count, HD), jnp.float32)
    (attended, attended_exact), unused = lax.scan(
        out_step, (zero_heads, zero_heads), (kv_blocks, pos_blocks), unroll=True
    )
    attended_low = (
        jnp.transpose(attended, (1, 0, 2)).reshape(row_count, head_count * HD).astype(jnp.bfloat16)
    )
    branch = lax.psum(jnp.dot(attended_low, wo_full, preferred_element_type=jnp.float32), "wsh")
    hidden = x_full + branch
    scale_two = lax.rsqrt(jnp.mean(hidden * hidden, axis=-1, keepdims=True) + epsilon)
    hat_two = hidden * scale_two
    normed_two = (hat_two * g_two).astype(jnp.bfloat16)
    gate_pre = jnp.dot(normed_two, wg_full, preferred_element_type=jnp.float32)
    up_proj = jnp.dot(normed_two, wu_full, preferred_element_type=jnp.float32)
    act_low = (jax.nn.silu(gate_pre) * up_proj).astype(jnp.bfloat16)
    mlp_out = lax.psum(
        jnp.dot(act_low, wd_full, preferred_element_type=jnp.float32).astype(jnp.bfloat16), "wsh"
    ).astype(jnp.float32)
    layer_out = (hidden + mlp_out).astype(jnp.bfloat16)
    wq_full, wkv_full, wo_full, wg_full, wu_full, wd_full = (
        lax.all_gather(w_query, ("seq", "ctx"), axis=0, tiled=True),
        lax.all_gather(w_keyvalue, ("seq", "ctx"), axis=0, tiled=True),
        lax.all_gather(w_output, ("seq", "ctx"), axis=1, tiled=True),
        lax.all_gather(w_gate, ("seq", "ctx"), axis=0, tiled=True),
        lax.all_gather(w_up, ("seq", "ctx"), axis=0, tiled=True),
        lax.all_gather(w_down, ("seq", "ctx"), axis=1, tiled=True),
    )
    grad_low = grad_out[0]
    grad_full = grad_low.astype(jnp.float32)
    grad_act = right_inner(grad_low, wd_full)
    gw_down_t = left_inner(grad_low, act_low)
    sigmoid_g = jax.nn.sigmoid(gate_pre)
    grad_up = (grad_act * (gate_pre * sigmoid_g)).astype(jnp.bfloat16)
    grad_gate = (grad_act * up_proj * sigmoid_g * (1.0 + gate_pre * (1.0 - sigmoid_g))).astype(
        jnp.bfloat16
    )
    gw_gate = left_inner(normed_two, grad_gate)
    gw_up = left_inner(normed_two, grad_up)
    part_two = right_inner(grad_gate, wg_full) + right_inner(grad_up, wu_full)
    gg_two = jnp.sum(part_two * hat_two, axis=0)
    grad_normed_two = lax.psum(part_two.astype(jnp.bfloat16), "wsh").astype(jnp.float32)
    grad_hidden = grad_full + norm_back(grad_normed_two, hat_two, scale_two, g_two)
    hidden_low = grad_hidden.astype(jnp.bfloat16)
    gw_out_t = left_inner(hidden_low, attended_low)
    grad_att = (
        right_inner(hidden_low, wo_full).reshape(row_count, head_count, HD).astype(jnp.bfloat16)
    )
    row_delta = jnp.sum(
        jnp.transpose(grad_att.astype(jnp.float32), (1, 0, 2)) * attended_exact, axis=-1
    )

    def back_step(grad_q, kv_pair):
        kv_block, pos_block = kv_pair
        scores = block_scores(kv_block, pos_block)
        prob_full = jnp.exp(scores - log_sum[..., None])
        prob_low = prob_full.astype(jnp.bfloat16)
        grad_prob = jnp.einsum(
            "qhd,kd->hqk", grad_att, kv_block[:, HD:], preferred_element_type=jnp.float32
        )
        grad_score = (prob_full * (grad_prob - row_delta[..., None])).astype(jnp.bfloat16)
        grad_q = grad_q + jnp.einsum(
            "hqk,kd->qhd", grad_score, kv_block[:, :HD], preferred_element_type=jnp.float32
        )
        grad_key = jnp.einsum(
            "hqk,qhd->kd", grad_score, query_low, preferred_element_type=jnp.float32
        )
        grad_value = jnp.einsum(
            "hqk,qhd->kd", prob_low, grad_att, preferred_element_type=jnp.float32
        )
        return (grad_q, jnp.concatenate([grad_key * score_scale, grad_value], axis=1))

    grad_q, kv_terms = lax.scan(
        back_step, jnp.zeros((row_count, head_count, HD), jnp.float32), (kv_blocks, pos_blocks),
        unroll=True,
    )
    grad_q = grad_q * score_scale
    grad_kv = lax.psum_scatter(
        kv_terms.reshape(seq_len, 2 * HD).astype(jnp.bfloat16),
        "ctx",
        scatter_dimension=0,
        tiled=True,
    ).astype(jnp.float32)
    grad_qpre = (
        rotate(grad_q, cos_tab, -sin_tab).reshape(row_count, head_count * HD).astype(jnp.bfloat16)
    )
    grad_kpre = rotate(grad_kv[:, None, :HD], cos_tab, -sin_tab)[:, 0, :]
    grad_kvpre = jnp.concatenate([grad_kpre, grad_kv[:, HD:]], axis=1).astype(jnp.bfloat16)
    gw_query = left_inner(normed_one, grad_qpre)
    gw_kv = left_inner(normed_one, grad_kvpre)
    wsh_count = lax.axis_size("wsh")
    gb_q_full = lax.dynamic_update_slice_in_dim(
        jnp.zeros((q_cols * wsh_count,), jnp.float32),
        jnp.sum(grad_qpre.astype(jnp.float32), axis=0),
        shard_id * q_cols,
        0,
    )
    gb_kv_full = lax.dynamic_update_slice_in_dim(
        jnp.zeros((kv_cols * wsh_count,), jnp.float32),
        jnp.sum(grad_kvpre.astype(jnp.float32), axis=0),
        shard_id * kv_cols,
        0,
    )
    part_one = right_inner(grad_qpre, wq_full) + right_inner(grad_kvpre, wkv_full)
    gg_one = jnp.sum(part_one * hat_one, axis=0)
    grad_normed_one = lax.psum(part_one.astype(jnp.bfloat16), "wsh").astype(jnp.float32)
    grad_input = (grad_hidden + norm_back(grad_normed_one, hat_one, scale_one, g_one)).astype(
        jnp.bfloat16
    )
    out_g_one, out_b_q, out_b_kv, out_g_two = (
        lax.psum_scatter(gg_one, ("seq", "ctx", "wsh"), scatter_dimension=0, tiled=True),
        lax.psum_scatter(gb_q_full, ("seq", "ctx", "wsh"), scatter_dimension=0, tiled=True),
        lax.psum_scatter(gb_kv_full, ("seq", "ctx", "wsh"), scatter_dimension=0, tiled=True),
        lax.psum_scatter(gg_two, ("seq", "ctx", "wsh"), scatter_dimension=0, tiled=True),
    )
    all_owned = lax.psum_scatter(
        jnp.concatenate(
            [gw_query, gw_kv, gw_out_t, gw_gate, gw_up, gw_down_t], axis=1
        ).astype(jnp.bfloat16),
        ("seq", "ctx"),
        scatter_dimension=0,
        tiled=True,
    ).astype(jnp.float32)
    proj_owned = all_owned[:, : 2 * q_cols + kv_cols]
    mlp_owned = all_owned[:, 2 * q_cols + kv_cols :]
    out_wq = proj_owned[:, :q_cols]
    out_wkv = proj_owned[:, q_cols : q_cols + kv_cols]
    out_wo = jnp.transpose(proj_owned[:, q_cols + kv_cols :])
    out_wg = mlp_owned[:, :ff_cols]
    out_wu = mlp_owned[:, ff_cols : 2 * ff_cols]
    out_wd = jnp.transpose(mlp_owned[:, 2 * ff_cols :])
    return (
        layer_out[None],
        grad_input[None],
        out_g_one,
        out_wq,
        out_b_q,
        out_wkv,
        out_b_kv,
        out_wo,
        out_g_two,
        out_wg,
        out_wu,
        out_wd,
    )


def solution(mesh):
    return jax.shard_map(
        per_device,
        mesh=mesh,
        in_specs=(
            P("seq", "ctx", None),
            P("seq", "ctx", None),
            P("seq", None),
            P(("seq", "ctx", "wsh")),
            P(("seq", "ctx"), "wsh"),
            P(("seq", "ctx", "wsh")),
            P(("seq", "ctx"), "wsh"),
            P(("seq", "ctx", "wsh")),
            P("wsh", ("seq", "ctx")),
            P(("seq", "ctx", "wsh")),
            P(("seq", "ctx"), "wsh"),
            P(("seq", "ctx"), "wsh"),
            P("wsh", ("seq", "ctx")),
        ),
        out_specs=(
            P("seq", "ctx", None),
            P("seq", "ctx", None),
            P(("seq", "ctx", "wsh")),
            P(("seq", "ctx"), "wsh"),
            P(("seq", "ctx", "wsh")),
            P(("seq", "ctx"), "wsh"),
            P(("seq", "ctx", "wsh")),
            P("wsh", ("seq", "ctx")),
            P(("seq", "ctx", "wsh")),
            P(("seq", "ctx"), "wsh"),
            P(("seq", "ctx"), "wsh"),
            P("wsh", ("seq", "ctx")),
        ),
        check_vma=False,
    )
```
